1024 devices in a mesh: section: 16 (over y, z_lo), dp: 64 (over x, z_hi, core).
Axes of the slice: x: 8, y: 8, z: 8 (z_hi: 4, z_lo: 2; z = z_hi * 2 + z_lo), core: 2. Of those that a mesh axis runs over, the one named last changes fastest.
Arguments:
- failed: int32 [64], P('dp'), may hold values from 0 to 15
- unfinished: int32 [64, 2], P('dp'), may hold values from 0 to 7, as said below
- lengths: int32 [64, 2], P('dp'), may hold values from 1 to 64
- acts: bfloat16 [16, 128, 64, 4096], P('section', 'dp'), may hold values from -100 to 100
- out_grads: bfloat16 [16, 512, 64, 512], P('section', 'dp'), may hold values from -30 to 30
- shadow_weight: bfloat16 [16, 4096, 512], P('section'), may hold values from -0.09375 to 0.09375
- shadow_gain: bfloat16 [16, 4096], P('section'), may hold values from 0.099609375 to 1.8984375
Outputs:
- in_grad: bfloat16 [16, 128, 64, 4096], P('section', 'dp')
- gain_grad: float32 [16, 4096], P('section', 'dp')
- bias_grad: float32 [16, 512], P('section', 'dp')
The draws below stay inside these ranges and needn't reach their ends.
Inputs may be any that keep to these rules, and one draw needn't show every extreme that they name: `unfinished`: in each replica's row the 2 ids differ.
All inputs are finite; a program needn't handle non-finite values.
Results may differ from the reference program's by a relative error of at most 0.001.
Values may be sent and summed in bfloat16 or wider, within the bound.
No kernel may reach another device: no remote copies, remote signals or barrier semaphores. Data moves between devices by JAX's collectives and lax.ppermute only.
A program may use at most 32 MiB of HBM per device.

```python
import math
import jax
import jax.numpy as jnp
from jax import lax

D = 4096
KVD = 512
MB = 2
MBALL = 8
SEQ = 64
N_SECTION = 16
N_DP = 64


def draw_failed(key, part):
    values = jax.random.randint(jax.random.fold_in(key, 5), (N_DP,), 0, N_SECTION)
    row_id = lax.broadcasted_iota(jnp.int32, (N_DP,), 0)
    values = jnp.where(row_id == 0, N_SECTION - 1, values)
    values = jnp.where(row_id == N_DP - 1, 0, values)
    return values.astype(jnp.int32)


def draw_unfinished(key, part):
    scores = jax.random.randint(key, (N_DP, MBALL), 0, 2 ** 20) * MBALL
    column = lax.broadcasted_iota(jnp.int32, (N_DP, MBALL), 1)
    row_id = lax.broadcasted_iota(jnp.int32, (N_DP, MBALL), 0)
    scores = scores + column
    scores = scores + jnp.where((row_id == 0) & (column == MBALL - 1), 2 ** 26, 0)
    scores = scores + jnp.where((row_id == N_DP - 1) & (column == 0), 2 ** 26, 0)
    order = jnp.argsort(-scores, axis=1, stable=True)
    return order[:, :MB].astype(jnp.int32)


def draw_lengths(key, part):
    values = jax.random.randint(key, (N_DP, MB), 1, SEQ + 1)
    row_id = lax.broadcasted_iota(jnp.int32, (N_DP, MB), 0)
    column = lax.broadcasted_iota(jnp.int32, (N_DP, MB), 1)
    values = jnp.where((row_id == 0) & (column == 0), SEQ, values)
    values = jnp.where((row_id == N_DP - 1) & (column == MB - 1), 1, values)
    return values.astype(jnp.int32)


def draw_acts(key, part):
    key_a, key_b, key_c = jax.random.split(jax.random.fold_in(key, 11), 3)
    shape = (N_SECTION, N_DP * MB, SEQ, D)
    base = jnp.clip(jax.random.normal(key_a, shape, jnp.float32), -4.0, 4.0)
    row_scale = jnp.exp(jax.random.uniform(key_b, (N_SECTION, N_DP * MB, SEQ, 1), jnp.float32, 0.0, math.log(10.0)))
    col_scale = jnp.exp(jax.random.uniform(key_c, (N_SECTION, 1, 1, D), jnp.float32, math.log(0.5), math.log(2.0)))
    return jnp.clip(base * row_scale * col_scale, -100.0, 100.0).astype(jnp.bfloat16)


def draw_out_grads(key, part):
    key_a = jax.random.fold_in(jax.random.fold_in(key, 23), 0)
    shape = (N_SECTION, N_DP * MBALL, SEQ, KVD)
    replica = (lax.broadcasted_iota(jnp.int32, (1, N_DP * MBALL, 1, 1), 1) // MBALL).astype(jnp.float32)
    spread_pos = replica / max(N_DP - 1, 1)
    base = jnp.clip(jax.random.normal(key_a, shape, jnp.float32), -4.0, 4.0)
    scale = jnp.exp(math.log(3.0) * spread_pos)
    return jnp.clip(base * scale, -30.0, 30.0).astype(jnp.bfloat16)


def shard_levels(key, extent, shards, low, high):
    factor_of = 1.0
    for position, parts in shards:
        steps = jax.random.uniform(jax.random.fold_in(jax.random.fold_in(key, 6), position), (parts,), jnp.float32, low / len(shards), high / len(shards))
        factor_of = factor_of * jnp.repeat(jnp.exp(steps), extent[position] // parts).reshape((-1,) + (1,) * (len(extent) - 1 - position))
    return factor_of


def noise(rng, shape, spread, bound, cuts=(), kind=jnp.bfloat16):
    values = spread * jax.random.normal(rng, shape, jnp.float32)
    if cuts:
        values = values * shard_levels(rng, shape, cuts, -0.22, 0.18)
    return jnp.clip(values, -bound, bound).astype(kind)


def setup_inputs(seed: int = 0) -> dict:
    keys = jax.random.split(jax.random.key(seed), 8)
    failed = draw_failed(jax.random.fold_in(keys[7], 71), 0)
    unfinished = draw_unfinished(jax.random.fold_in(keys[7], 71), 0)
    lengths = draw_lengths(jax.random.fold_in(keys[7], 71), 0)
    acts = draw_acts(jax.random.fold_in(keys[7], 71), 0)
    out_grads = draw_out_grads(jax.random.fold_in(keys[7], 71), 0)
    shadow_weight = noise(keys[5], (N_SECTION, D, KVD), D ** -0.5, 0.09375, ((0, 16),))
    shadow_gain = jnp.clip(1.0 + 0.18 * jax.random.normal(keys[6], (N_SECTION, D), jnp.float32), 0.099609375, 1.8984375).astype(jnp.bfloat16)
    return dict(failed=failed, unfinished=unfinished, lengths=lengths, acts=acts, out_grads=out_grads, shadow_weight=shadow_weight, shadow_gain=shadow_gain)


EPSILON = 1e-06

def reference(failed, unfinished, lengths, acts, out_grads, shadow_weight, shadow_gain):
    helper = (failed + N_SECTION - 1) % N_SECTION
    source = (failed + 1) % N_SECTION
    replica_ids = jnp.arange(N_DP, dtype=jnp.int32)

    def one_replica(rep, help_section, src_section, picked_ids, live_len):
        rows = lax.dynamic_slice_in_dim(lax.dynamic_index_in_dim(acts, help_section, 0, keepdims=False), (rep * MB).astype(jnp.int32), MB, 0).reshape(MB * SEQ, D)
        sent = lax.dynamic_slice_in_dim(lax.dynamic_index_in_dim(out_grads, src_section, 0, keepdims=False), (rep * MBALL).astype(jnp.int32), MBALL, 0)
        picked = jnp.take(sent, picked_ids, axis=0)
        live = jnp.arange(SEQ, dtype=jnp.int32)[None, :] < live_len[:, None]
        grads = jnp.where(live[..., None], picked, jnp.zeros_like(picked)).reshape(MB * SEQ, KVD)
        weight = lax.dynamic_index_in_dim(shadow_weight, help_section, 0, keepdims=False)
        gain = lax.dynamic_index_in_dim(shadow_gain, help_section, 0, keepdims=False).astype(jnp.float32)
        wide = rows.astype(jnp.float32)
        inv_rms = lax.rsqrt(lax.optimization_barrier(jnp.mean(wide * wide, axis=1, keepdims=True)) + EPSILON)
        normed = wide * inv_rms
        grad_norm = jnp.dot(grads, weight.T, preferred_element_type=jnp.float32)
        grad_hat = grad_norm * gain[None, :]
        inner = lax.optimization_barrier(jnp.mean(grad_hat * normed, axis=1, keepdims=True))
        dx = inv_rms * (grad_hat - normed * inner)
        gain_row = lax.optimization_barrier(jnp.sum(grad_norm * normed, axis=0)) / N_DP
        bias_row = lax.optimization_barrier(jnp.sum(grads.astype(jnp.float32), axis=0)) / N_DP
        return (dx.astype(jnp.bfloat16).reshape(MB, SEQ, D), gain_row, bias_row)
    dx_all, gain_rows, bias_rows = lax.map(lambda a: one_replica(*a), (replica_ids, helper, source, unfinished, lengths))
    section_ids = jnp.arange(N_SECTION, dtype=jnp.int32)
    hit = section_ids[:, None] == helper[None, :]
    dx_flat = dx_all.reshape(N_DP * MB, SEQ, D)
    hit_rows = jnp.repeat(hit, MB, axis=1)
    in_grad = jnp.where(hit_rows[:, :, None, None], dx_flat[None], jnp.zeros((), jnp.bfloat16))
    weights = hit.astype(jnp.float32)
    gain_grad = jnp.dot(weights, gain_rows, precision=lax.Precision.HIGHEST)
    bias_grad = jnp.dot(weights, bias_rows, precision=lax.Precision.HIGHEST)
    return (in_grad, gain_grad, bias_grad)
```

```python
import jax
import jax.numpy as jnp
from jax import lax
from jax.sharding import PartitionSpec as P

EPSILON = 1e-06


def local_backward(rows, grads, weight, gain, replicas):
    wide = rows.astype(jnp.float32)
    inv_rms = lax.rsqrt(jnp.mean(wide * wide, axis=1, keepdims=True) + EPSILON)
    normed = wide * inv_rms
    grad_norm = lax.dot_general(
        grads, weight, (((1,), (1,)), ((), ())), preferred_element_type=jnp.float32
    )
    grad_hat = grad_norm * gain.astype(jnp.float32)[None, :]
    inner = jnp.mean(grad_hat * normed, axis=1, keepdims=True)
    result = (inv_rms * (grad_hat - normed * inner)).astype(jnp.bfloat16)
    gain_part = jnp.sum(grad_norm * normed, axis=0) / replicas
    bias_part = jnp.sum(grads.astype(jnp.float32), axis=0) / replicas
    return (result, gain_part, bias_part)


def reduce_over_dp(parts):
    got = lax.all_to_all(parts, "dp", 0, 0, tiled=True)
    return jnp.sum(got, axis=0, keepdims=True)


def per_device(failed, unfinished, lengths, acts, out_grads, shadow_weight, shadow_gain):
    sections = lax.axis_size("section")
    replicas = lax.axis_size("dp")
    helper = (failed[0] + sections - 1) % sections
    on_helper = lax.axis_index("section") == helper
    picked_ids = unfinished[0]
    live_len = lengths[0]
    slot_count, seq_len, channels = acts.shape[1], acts.shape[2], acts.shape[3]
    features = out_grads.shape[3]
    total_rows = slot_count * seq_len
    chosen = jnp.take(out_grads[0], picked_ids, axis=0)
    position = lax.broadcasted_iota(jnp.int32, chosen.shape[:2], 1)
    chosen = jnp.where((position < live_len[:, None])[..., None], chosen, jnp.zeros_like(chosen))
    pairs = [(s, (s - 2) % sections) for s in range(sections)]
    grads = lax.ppermute(chosen, "section", pairs)
    collected, gain_part, bias_part = local_backward(
        acts[0].reshape(total_rows, channels),
        grads.reshape(total_rows, features),
        shadow_weight[0], shadow_gain[0], replicas)
    collected = jnp.where(on_helper, collected, jnp.zeros_like(collected))
    gain_part = jnp.where(on_helper, gain_part, jnp.zeros_like(gain_part))
    bias_part = jnp.where(on_helper, bias_part, jnp.zeros_like(bias_part))
    parts = jnp.concatenate([gain_part.reshape(replicas, -1), bias_part.reshape(replicas, -1)], axis=1)
    mine = reduce_over_dp(parts)
    gw = channels // replicas
    in_grad = collected.reshape(1, slot_count, seq_len, channels)
    return (in_grad, mine[:, :gw], mine[:, gw:])


def solution(mesh):
    in_specs = (P("dp"), P("dp", None), P("dp", None), P("section", "dp", None, None),
                P("section", "dp", None, None), P("section", None, None), P("section", None))
    out_specs = (P("section", "dp", None, None), P("section", "dp"), P("section", "dp"))
    return jax.shard_map(per_device, mesh=mesh, in_specs=in_specs, out_specs=out_specs, check_vma=False)
```

```python
import jax
import jax.numpy as jnp
from jax import lax
from jax.experimental import pallas as pl
from jax.experimental.pallas import tpu as pltpu
from jax.sharding import PartitionSpec as P

EPSILON = 1e-06
BLOCK = 512


def terms_kernel(g_ref, keep_ref, a_ref, r_ref, w_ref, gain_ref, bias_ref):
    g = jnp.where(keep_ref[...] > 0, g_ref[...], jnp.zeros_like(g_ref[...]))
    bias_ref[...] = jnp.sum(g.astype(jnp.float32), axis=0, keepdims=True)
    inv_rms = r_ref[...]
    for j in range(a_ref.shape[1] // BLOCK):
        cols = slice(j * BLOCK, (j + 1) * BLOCK)
        grad_norm = lax.dot_general(
            g, w_ref[cols, :], (((1,), (1,)), ((), ())), preferred_element_type=jnp.float32
        )
        normed = a_ref[:, cols].astype(jnp.float32) * inv_rms
        gain_ref[:, cols] = jnp.sum(grad_norm * normed, axis=0, keepdims=True)


def reduction_terms(grads, keep, rows, inv_rms, weight):
    tokens, features = grads.shape
    channels = rows.shape[1]
    vmem = pl.BlockSpec(memory_space=pltpu.VMEM)
    return pl.pallas_call(
        terms_kernel,
        out_shape=(
            jax.ShapeDtypeStruct((1, channels), jnp.float32),
            jax.ShapeDtypeStruct((1, features), jnp.float32),
        ),
        in_specs=[vmem] * 5,
        out_specs=(vmem, vmem),
        cost_estimate=pl.CostEstimate(
            flops=2 * tokens * features * channels,
            bytes_accessed=2 * (channels * features + tokens * channels + tokens * features),
            transcendentals=0,
        ),
    )(grads, keep, rows, inv_rms, weight)


def per_device(failed, unfinished, lengths, acts, out_grads, shadow_weight, shadow_gain):
    sections = lax.axis_size("section")
    replicas = lax.axis_size("dp")
    helper = (failed[0] + sections - 1) % sections
    on_helper = lax.axis_index("section") == helper
    picked_ids = unfinished[0]
    live_len = lengths[0]
    slot_count, seq_len, channels = acts.shape[1], acts.shape[2], acts.shape[3]
    features = out_grads.shape[3]
    total_rows = slot_count * seq_len

    chosen = jnp.take(out_grads[0], picked_ids, axis=0)
    pairs = [(s, (s - 2) % sections) for s in range(sections)]
    grads = lax.ppermute(chosen, "section", pairs).reshape(total_rows, features)
    position = lax.broadcasted_iota(jnp.int32, (slot_count, seq_len), 1)
    live = (position < live_len[:, None]).reshape(total_rows, 1)

    rows = acts[0].reshape(total_rows, channels)
    wide = rows.astype(jnp.float32)
    inv_rms = lax.rsqrt(jnp.mean(wide * wide, axis=1, keepdims=True) + EPSILON)
    weight = shadow_weight[0]

    gain_sum, bias_sum = reduction_terms(grads, live.astype(jnp.float32), rows, inv_rms, weight)
    gain_part = jnp.where(on_helper, gain_sum / replicas, 0.0)
    bias_part = jnp.where(on_helper, bias_sum / replicas, 0.0)
    parts = jnp.concatenate(
        [gain_part.reshape(replicas, -1), bias_part.reshape(replicas, -1)], axis=1
    )
    mine = jnp.sum(lax.all_to_all(parts, "dp", 0, 0, tiled=True), axis=0, keepdims=True)

    masked = jnp.where(live, grads, jnp.zeros_like(grads))
    normed = wide * inv_rms
    grad_norm = lax.dot_general(
        masked, weight, (((1,), (1,)), ((), ())), preferred_element_type=jnp.float32
    )
    grad_hat = grad_norm * shadow_gain[0].astype(jnp.float32)[None, :]
    inner = jnp.mean(grad_hat * normed, axis=1, keepdims=True)
    dx = (inv_rms * (grad_hat - normed * inner)).astype(jnp.bfloat16)
    dx = jnp.where(on_helper, dx, jnp.zeros_like(dx))

    width = channels // replicas
    in_grad = dx.reshape(1, slot_count, seq_len, channels)
    return (in_grad, mine[:, :width], mine[:, width:])


def solution(mesh):
    in_specs = (
        P("dp"),
        P("dp", None),
        P("dp", None),
        P("section", "dp", None, None),
        P("section", "dp", None, None),
        P("section", None, None),
        P("section", None),
    )
    out_specs = (P("section", "dp", None, None), P("section", "dp"), P("section", "dp"))
    return jax.shard_map(
        per_device, mesh=mesh, in_specs=in_specs, out_specs=out_specs, check_vma=False
    )
```

```python
import jax
import jax.numpy as jnp
from jax import lax
from jax.sharding import PartitionSpec as P

EPSILON = 1e-06


def local_backward(rows, grads, weight, gain, replicas):
    wide = rows.astype(jnp.float32)
    inv_rms = lax.rsqrt(jnp.mean(wide * wide, axis=1, keepdims=True) + EPSILON)
    normed = wide * inv_rms
    grad_norm = lax.dot_general(
        grads, weight, (((1,), (1,)), ((), ())), preferred_element_type=jnp.float32
    )
    grad_hat = grad_norm * gain.astype(jnp.float32)[None, :]
    inner = jnp.mean(grad_hat * normed, axis=1, keepdims=True)
    result = (inv_rms * (grad_hat - normed * inner)).astype(jnp.bfloat16)
    gain_part = jnp.sum(grad_norm * normed, axis=0) / replicas
    bias_part = jnp.sum(grads.astype(jnp.float32), axis=0) / replicas
    return (result, gain_part, bias_part)


def reduce_over_dp(parts):
    got = lax.all_to_all(parts, "dp", 0, 0, tiled=True)
    return jnp.sum(got, axis=0, keepdims=True)


def per_device(failed, unfinished, lengths, acts, out_grads, shadow_weight, shadow_gain):
    sections = lax.axis_size("section")
    replicas = lax.axis_size("dp")
    helper = (failed[0] + sections - 1) % sections
    on_helper = lax.axis_index("section") == helper
    picked_ids = unfinished[0]
    live_len = lengths[0]
    slot_count, seq_len, channels = acts.shape[1], acts.shape[2], acts.shape[3]
    features = out_grads.shape[3]
    total_rows = slot_count * seq_len
    chosen = jnp.take(out_grads[0], picked_ids, axis=0, mode="clip")
    pairs = [(s, (s - 2) % sections) for s in range(sections)]
    grads = lax.ppermute(chosen, "section", pairs)
    position = lax.broadcasted_iota(jnp.int32, grads.shape[:2], 1)
    grads = jnp.where((position < live_len[:, None])[..., None], grads, jnp.zeros_like(grads))
    collected, gain_part, bias_part = local_backward(
        acts[0].reshape(total_rows, channels),
        grads.reshape(total_rows, features),
        shadow_weight[0], shadow_gain[0], replicas)
    collected = jnp.where(on_helper, collected, jnp.zeros_like(collected))
    gain_part = jnp.where(on_helper, gain_part, jnp.zeros_like(gain_part))
    bias_part = jnp.where(on_helper, bias_part, jnp.zeros_like(bias_part))
    parts = jnp.concatenate([gain_part.reshape(replicas, -1), bias_part.reshape(replicas, -1)], axis=1)
    mine = reduce_over_dp(parts)
    gw = channels // replicas
    in_grad = collected.reshape(1, slot_count, seq_len, channels)
    return (in_grad, mine[:, :gw], mine[:, gw:])


def solution(mesh):
    in_specs = (P("dp"), P("dp", None), P("dp", None), P("section", "dp", None, None),
                P("section", "dp", None, None), P("section", None, None), P("section", None))
    out_specs = (P("section", "dp", None, None), P("section", "dp"), P("section", "dp"))
    return jax.shard_map(per_device, mesh=mesh, in_specs=in_specs, out_specs=out_specs, check_vma=False)
```

```python
import jax
import jax.numpy as jnp
from jax import lax
from jax.sharding import PartitionSpec as P

EPSILON = 1e-06


def local_backward(rows, grads, weight, gain, replicas):
    wide = rows.astype(jnp.float32)
    inv_rms = lax.rsqrt(jnp.mean(wide * wide, axis=1, keepdims=True) + EPSILON)
    normed = wide * inv_rms
    grad_norm = lax.dot_general(
        grads, weight, (((1,), (1,)), ((), ())), preferred_element_type=jnp.float32
    )
    grad_hat = grad_norm * gain.astype(jnp.float32)[None, :]
    inner = jnp.mean(grad_hat * normed, axis=1, keepdims=True)
    result = (inv_rms * (grad_hat - normed * inner)).astype(jnp.bfloat16)
    gain_part = jnp.sum(grad_norm * normed, axis=0) / replicas
    bias_part = jnp.sum(grads.astype(jnp.float32), axis=0) / replicas
    return (result, gain_part, bias_part)


def reduce_over_dp(parts, width):
    got = lax.all_to_all(parts, "dp", 0, 0, tiled=True)
    return (jnp.sum(got[:, :width], axis=0, keepdims=True), jnp.sum(got[:, width:], axis=0, keepdims=True))


def per_device(failed, unfinished, lengths, acts, out_grads, shadow_weight, shadow_gain):
    sections = lax.axis_size("section")
    replicas = lax.axis_size("dp")
    helper = (failed[0] + sections - 1) % sections
    on_helper = lax.axis_index("section") == helper
    picked_ids = unfinished[0]
    live_len = lengths[0]
    slot_count, seq_len, channels = acts.shape[1], acts.shape[2], acts.shape[3]
    features = out_grads.shape[3]
    total_rows = slot_count * seq_len
    chosen = jnp.take(out_grads[0], picked_ids, axis=0, mode="clip")
    pairs = [(s, (s - 2) % sections) for s in range(sections)]
    grads = lax.ppermute(chosen, "section", pairs)
    position = lax.broadcasted_iota(jnp.int32, grads.shape[:2], 1)
    grads = jnp.where((position < live_len[:, None])[..., None], grads, jnp.zeros_like(grads))
    collected, gain_part, bias_part = local_backward(
        acts[0].reshape(total_rows, channels),
        grads.reshape(total_rows, features),
        shadow_weight[0], shadow_gain[0], replicas)
    collected = jnp.where(on_helper, collected, jnp.zeros_like(collected))
    gain_part = jnp.where(on_helper, gain_part, jnp.zeros_like(gain_part))
    bias_part = jnp.where(on_helper, bias_part, jnp.zeros_like(bias_part))
    parts = jnp.concatenate([gain_part.reshape(replicas, -1), bias_part.reshape(replicas, -1)], axis=1)
    gw = channels // replicas
    in_grad = collected.reshape(1, slot_count, seq_len, channels)
    gain_share, bias_share = reduce_over_dp(parts, gw)
    return (in_grad, gain_share, bias_share)


def solution(mesh):
    in_specs = (P("dp"), P("dp", None), P("dp", None), P("section", "dp", None, None),
                P("section", "dp", None, None), P("section", None, None), P("section", None))
    out_specs = (P("section", "dp", None, None), P("section", "dp"), P("section", "dp"))
    return jax.shard_map(per_device, mesh=mesh, in_specs=in_specs, out_specs=out_specs, check_vma=False)
```

```python
import jax
import jax.numpy as jnp
from jax import lax
from jax.sharding import PartitionSpec as P

EPSILON = 1e-06


def reduction_terms(rows, inv_rms, grads, weight, replicas):
    wide = rows.astype(jnp.float32)
    normed = wide * inv_rms
    grad_norm = lax.dot_general(
        grads, weight, (((1,), (1,)), ((), ())), preferred_element_type=jnp.float32
    )
    gain_part = jnp.sum(grad_norm * normed, axis=0) / replicas
    bias_part = jnp.sum(grads.astype(jnp.float32), axis=0) / replicas
    return (gain_part, bias_part)


def input_grad(rows, inv_rms, grads, weight, gain):
    wide = rows.astype(jnp.float32)
    normed = wide * inv_rms
    grad_norm = lax.dot_general(
        grads, weight, (((1,), (1,)), ((), ())), preferred_element_type=jnp.float32
    )
    grad_hat = grad_norm * gain.astype(jnp.float32)[None, :]
    inner = jnp.mean(grad_hat * normed, axis=1, keepdims=True)
    return (inv_rms * (grad_hat - normed * inner)).astype(jnp.bfloat16)


def reduce_over_dp(parts):
    got = lax.all_to_all(parts, "dp", 0, 0, tiled=True)
    return jnp.sum(got, axis=0, keepdims=True)


def per_device(failed, unfinished, lengths, acts, out_grads, shadow_weight, shadow_gain):
    sections = lax.axis_size("section")
    replicas = lax.axis_size("dp")
    helper = (failed[0] + sections - 1) % sections
    on_helper = lax.axis_index("section") == helper
    picked_ids = unfinished[0]
    live_len = lengths[0]
    slot_count, seq_len, channels = acts.shape[1], acts.shape[2], acts.shape[3]
    features = out_grads.shape[3]
    total_rows = slot_count * seq_len
    chosen = jnp.take(out_grads[0], picked_ids, axis=0, mode="clip")
    pairs = [(s, (s - 2) % sections) for s in range(sections)]
    grads = lax.ppermute(chosen, "section", pairs)
    position = lax.broadcasted_iota(jnp.int32, grads.shape[:2], 1)
    grads = jnp.where((position < live_len[:, None])[..., None], grads, jnp.zeros_like(grads))
    rows = acts[0].reshape(total_rows, channels)
    grads = grads.reshape(total_rows, features)
    wide = rows.astype(jnp.float32)
    inv_rms = lax.rsqrt(jnp.mean(wide * wide, axis=1, keepdims=True) + EPSILON)
    gain_part, bias_part = reduction_terms(rows, inv_rms, grads, shadow_weight[0], replicas)
    gain_part = jnp.where(on_helper, gain_part, jnp.zeros_like(gain_part))
    bias_part = jnp.where(on_helper, bias_part, jnp.zeros_like(bias_part))
    parts = jnp.concatenate([gain_part.reshape(replicas, -1), bias_part.reshape(replicas, -1)], axis=1)
    late_rows, late_inv, late_grads, parts = lax.optimization_barrier((rows, inv_rms, grads, parts))
    mine = reduce_over_dp(parts)
    collected = input_grad(late_rows, late_inv, late_grads, shadow_weight[0], shadow_gain[0])
    collected = jnp.where(on_helper, collected, jnp.zeros_like(collected))
    gw = channels // replicas
    in_grad = collected.reshape(1, slot_count, seq_len, channels)
    return (in_grad, mine[:, :gw], mine[:, gw:])


def solution(mesh):
    in_specs = (P("dp"), P("dp", None), P("dp", None), P("section", "dp", None, None),
                P("section", "dp", None, None), P("section", None, None), P("section", None))
    out_specs = (P("section", "dp", None, None), P("section", "dp"), P("section", "dp"))
    return jax.shard_map(per_device, mesh=mesh, in_specs=in_specs, out_specs=out_specs, check_vma=False)
```

```python
import jax
import jax.numpy as jnp
from jax import lax
from jax.sharding import PartitionSpec as P

EPSILON = 1e-06


def reduction_terms(rows, inv_rms, grads, weight, replicas):
    wide = rows.astype(jnp.float32)
    normed = wide * inv_rms
    grad_norm = lax.dot_general(
        grads, weight, (((1,), (1,)), ((), ())), preferred_element_type=jnp.float32
    )
    gain_part = jnp.sum(grad_norm * normed, axis=0) / replicas
    bias_part = jnp.sum(grads.astype(jnp.float32), axis=0) / replicas
    return (gain_part, bias_part)


def input_grad(rows, inv_rms, grads, weight, gain):
    wide = rows.astype(jnp.float32)
    normed = wide * inv_rms
    grad_norm = lax.dot_general(
        grads, weight, (((1,), (1,)), ((), ())), preferred_element_type=jnp.float32
    )
    grad_hat = grad_norm * gain.astype(jnp.float32)[None, :]
    inner = jnp.mean(grad_hat * normed, axis=1, keepdims=True)
    return (inv_rms * (grad_hat - normed * inner)).astype(jnp.bfloat16)


def reduce_over_dp(parts):
    got = lax.all_to_all(parts, "dp", 0, 0, tiled=True)
    return jnp.sum(got, axis=0, keepdims=True)


def per_device(failed, unfinished, lengths, acts, out_grads, shadow_weight, shadow_gain):
    sections = lax.axis_size("section")
    replicas = lax.axis_size("dp")
    helper = (failed[0] + sections - 1) % sections
    on_helper = lax.axis_index("section") == helper
    picked_ids = unfinished[0]
    live_len = lengths[0]
    slot_count, seq_len, channels = acts.shape[1], acts.shape[2], acts.shape[3]
    features = out_grads.shape[3]
    total_rows = slot_count * seq_len
    chosen = jnp.take(out_grads[0], picked_ids, axis=0, mode="clip")
    pairs = [(s, (s - 2) % sections) for s in range(sections)]
    grads = lax.ppermute(chosen, "section", pairs)
    position = lax.broadcasted_iota(jnp.int32, grads.shape[:2], 1)
    grads = jnp.where((position < live_len[:, None])[..., None], grads, jnp.zeros_like(grads))
    rows = acts[0].reshape(total_rows, channels)
    grads = grads.reshape(total_rows, features)
    wide = rows.astype(jnp.float32)
    squares = lax.dot_general(rows, rows, (((1,), (1,)), ((), ())), preferred_element_type=jnp.float32)
    eye = lax.broadcasted_iota(jnp.int32, squares.shape, 0) == lax.broadcasted_iota(jnp.int32, squares.shape, 1)
    sum_sq = jnp.sum(jnp.where(eye, squares, 0.0), axis=1, keepdims=True)
    inv_rms = lax.rsqrt(sum_sq / channels + EPSILON)
    gain_part, bias_part = reduction_terms(rows, inv_rms, grads, shadow_weight[0], replicas)
    gain_part = jnp.where(on_helper, gain_part, jnp.zeros_like(gain_part))
    bias_part = jnp.where(on_helper, bias_part, jnp.zeros_like(bias_part))
    parts = jnp.concatenate([gain_part.reshape(replicas, -1), bias_part.reshape(replicas, -1)], axis=1)
    late_rows, late_inv, late_grads, parts = lax.optimization_barrier((rows, inv_rms, grads, parts))
    mine = reduce_over_dp(parts)
    collected = input_grad(late_rows, late_inv, late_grads, shadow_weight[0], shadow_gain[0])
    collected = jnp.where(on_helper, collected, jnp.zeros_like(collected))
    gw = channels // replicas
    in_grad = collected.reshape(1, slot_count, seq_len, channels)
    return (in_grad, mine[:, :gw], mine[:, gw:])


def solution(mesh):
    in_specs = (P("dp"), P("dp", None), P("dp", None), P("section", "dp", None, None),
                P("section", "dp", None, None), P("section", None, None), P("section", None))
    out_specs = (P("section", "dp", None, None), P("section", "dp"), P("section", "dp"))
    return jax.shard_map(per_device, mesh=mesh, in_specs=in_specs, out_specs=out_specs, check_vma=False)
```
